256 devices in a mesh: gz: 32 (over x, z), gx: 8 (over y, core).
Axes of the slice: x: 4, y: 4, z: 8, core: 2. Of those that a mesh axis runs over, the one named last changes fastest.
Arguments:
- u_field: bfloat16 [2, 512, 2048, 128], P(None, 'gx', 'gz'), may hold values from -64 to 64, as said below
- w_field: bfloat16 [2, 512, 2048, 128], P(None, 'gx', 'gz'), may hold values from -64 to 64, as said below
Outputs:
- modes: float32 [2, 512, 2048, 128], P(None, 'gx', 'gz')
- factor_r: float32 [2, 128, 128], replicated
The draws below stay inside these ranges and needn't reach their ends.
Inputs may be any that keep to these rules, and one draw needn't show every extreme that they name: `u_field`: velocity values of a snapshot. `w_field`: velocity values of a snapshot.
All inputs are finite; a program needn't handle non-finite values.
Results may differ from the reference program's by a relative error of at most 0.0003.
Values may be sent and summed in bfloat16 or wider, within the bound.
No kernel may reach another device: no remote copies, remote signals or barrier semaphores. Data moves between devices by JAX's collectives and lax.ppermute only.
A program may use at most 64 MiB of HBM per device.

```python
import jax
import jax.numpy as jnp
from jax import lax

SNAPS = 128
PLANES = 2
NX = 512
NZ = 2048


def rough_field(key):
    keys = jax.random.split(key, 3)
    shape = (PLANES, NX, NZ, SNAPS)
    base = jax.random.normal(keys[0], shape, jnp.float32)
    rise = 3.0
    column_scale = jnp.exp(jax.random.uniform(keys[1], (SNAPS,), jnp.float32, 0.0, 2.302585))
    row_scale = jnp.exp(jax.random.uniform(keys[2], (PLANES, NX, NZ, 1), jnp.float32, 0.0, 2.302585))
    along_x = jnp.arange(NX, dtype=jnp.float32) / NX
    along_z = jnp.arange(NZ, dtype=jnp.float32) / NZ
    trend = rise ** (along_x[:, None] + along_z[None, :])
    values = 0.05 * base * column_scale * row_scale * trend[None, :, :, None]
    return jnp.clip(values, -64.0, 64.0)


def draw_u_field(key, part):
    return rough_field(jax.random.fold_in(key, 11)).astype(jnp.bfloat16)


def draw_w_field(key, part):
    return rough_field(jax.random.fold_in(key, 23)).astype(jnp.bfloat16)


def setup_inputs(seed: int = 0) -> dict:
    arg_keys = jax.random.split(jax.random.key(seed), 3)
    return {
        "u_field": draw_u_field(jax.random.fold_in(arg_keys[2], 71), 0),
        "w_field": draw_w_field(jax.random.fold_in(arg_keys[2], 71), 0),
    }


span_step = 0.75

def derivative(field, axis_number):
    ahead_one = jnp.roll(field, -1, axis_number)
    behind_one = jnp.roll(field, 1, axis_number)
    ahead_two = jnp.roll(field, -2, axis_number)
    behind_two = jnp.roll(field, 2, axis_number)
    return 8.0 * (ahead_one - behind_one) - (ahead_two - behind_two)

def one_plane(plane_pair):
    u_plane = plane_pair[0].astype(jnp.float32)
    w_plane = plane_pair[1].astype(jnp.float32)
    vorticity = derivative(u_plane, 1) / (12.0 * span_step) - derivative(w_plane, 0) / 12.0
    columns = vorticity.reshape(NX * NZ, SNAPS)
    gram = jnp.dot(columns.T.astype(jnp.float32), columns.astype(jnp.float32), precision=lax.Precision.HIGHEST, preferred_element_type=jnp.float32) / (NX * NZ)
    lower = jnp.linalg.cholesky(gram)
    identity_matrix = jnp.eye(SNAPS, dtype=gram.dtype)
    inverse_r = lax.linalg.triangular_solve(lower, identity_matrix, left_side=True, lower=True).T
    modes = jnp.dot(columns.astype(jnp.float32), inverse_r.astype(jnp.float32), precision=lax.Precision.HIGHEST, preferred_element_type=jnp.float32)
    return (modes.reshape(NX, NZ, SNAPS), lower.T)

def reference(u_field, w_field):
    modes, factor_r = lax.map(one_plane, (u_field, w_field))
    return (modes, factor_r)
```

```python
import jax
import jax.numpy as jnp
from jax import lax
from jax.sharding import PartitionSpec as P

span_step = 0.75


def with_halo(cells, sides, width):
    for axis, dim in sides:
        count = lax.axis_size(axis)
        head = lax.slice_in_dim(cells, 0, width, axis=dim)
        tail = lax.slice_in_dim(cells, cells.shape[dim] - width, cells.shape[dim], axis=dim)
        cells = jnp.concatenate(
            [
                lax.ppermute(tail, axis, [(i, (i + 1) % count) for i in range(count)]),
                cells,
                lax.ppermute(head, axis, [((i + 1) % count, i) for i in range(count)]),
            ],
            axis=dim,
        )
    return cells


def butterfly_sum(x, axes):
    for axis in axes:
        count = lax.axis_size(axis)
        step = 1
        while step < count:
            x = x + lax.ppermute(x, axis, [(i, i ^ step) for i in range(count)])
            step *= 2
    return x


def pack_pair(gram):
    n = gram.shape[-1]
    row = lax.broadcasted_iota(jnp.int32, (n, n), 0)
    col = lax.broadcasted_iota(jnp.int32, (n, n), 1)
    square = jnp.where(row <= col, gram[0], gram[1])
    diag = jnp.diagonal(gram[1])[None, :]
    pad = jnp.zeros((7, n), gram.dtype)
    return jnp.concatenate([square, diag, pad], axis=0)


def unpack_pair(packed):
    n = packed.shape[-1]
    square = packed[:n]
    diag = packed[n]
    row = lax.broadcasted_iota(jnp.int32, (n, n), 0)
    col = lax.broadcasted_iota(jnp.int32, (n, n), 1)
    flipped = square.T
    first = jnp.where(row <= col, square, flipped)
    second = jnp.where(row > col, square, jnp.where(row < col, flipped, jnp.diag(diag)))
    return jnp.stack([first, second])


def local(u_field, w_field):
    planes, rows_x, rows_z, snaps = u_field.shape
    padded_u = with_halo(u_field, (("gz", 2),), 2).astype(jnp.float32)
    padded_w = with_halo(w_field, (("gx", 1),), 2).astype(jnp.float32)
    span_diff = 8.0 * (padded_u[:, :, 3:-1] - padded_u[:, :, 1:-3]) - (
        padded_u[:, :, 4:] - padded_u[:, :, :-4]
    )
    stream_diff = 8.0 * (padded_w[:, 3:-1] - padded_w[:, 1:-3]) - (
        padded_w[:, 4:] - padded_w[:, :-4]
    )
    vorticity = span_diff / (12.0 * span_step) - stream_diff / 12.0
    columns = vorticity.reshape(planes, rows_x * rows_z, snaps)
    gram_local = jnp.einsum(
        "pcs,pct->pst",
        columns,
        columns,
        precision=lax.Precision.HIGHEST,
        preferred_element_type=jnp.float32,
    )
    if planes == 2:
        gram_sum = unpack_pair(butterfly_sum(pack_pair(gram_local), ("gx", "gz")))
    else:
        gram_sum = butterfly_sum(gram_local, ("gx", "gz"))
    total_cells = rows_x * rows_z * lax.axis_size("gz") * lax.axis_size("gx")
    gram = gram_sum / total_cells
    lower = jnp.linalg.cholesky(gram)
    identity_matrix = jnp.broadcast_to(jnp.eye(snaps, dtype=gram.dtype), lower.shape)
    lower_inverse = lax.linalg.triangular_solve(lower, identity_matrix, left_side=True, lower=True)
    inverse_r = jnp.transpose(lower_inverse, (0, 2, 1))
    modes = jnp.einsum(
        "pcs,pst->pct",
        columns,
        inverse_r,
        precision=lax.Precision.HIGHEST,
        preferred_element_type=jnp.float32,
    )
    modes = modes.reshape(planes, rows_x, rows_z, snaps)
    factor_r = jnp.transpose(lower, (0, 2, 1))
    return (modes, factor_r)


def solution(mesh):
    return jax.shard_map(
        local,
        mesh=mesh,
        in_specs=(P(None, "gx", "gz", None), P(None, "gx", "gz", None)),
        out_specs=(P(None, "gx", "gz", None), P()),
        check_vma=False,
    )
```

```python
import jax
import jax.numpy as jnp
from jax import lax
from jax.experimental import pallas as pl
from jax.experimental.pallas import tpu as pltpu
from jax.sharding import PartitionSpec as P

span_step = 0.75


def with_halo(cells, sides, width):
    for axis, dim in sides:
        count = lax.axis_size(axis)
        head = lax.slice_in_dim(cells, 0, width, axis=dim)
        tail = lax.slice_in_dim(cells, cells.shape[dim] - width, cells.shape[dim], axis=dim)
        cells = jnp.concatenate(
            [
                lax.ppermute(tail, axis, [(i, (i + 1) % count) for i in range(count)]),
                cells,
                lax.ppermute(head, axis, [((i + 1) % count, i) for i in range(count)]),
            ],
            axis=dim,
        )
    return cells


def butterfly_sum(x, axes):
    for axis in axes:
        count = lax.axis_size(axis)
        step = 1
        while step < count:
            x = x + lax.ppermute(x, axis, [(i, i ^ step) for i in range(count)])
            step *= 2
    return x


def pack_pair(gram):
    n = gram.shape[-1]
    row = lax.broadcasted_iota(jnp.int32, (n, n), 0)
    col = lax.broadcasted_iota(jnp.int32, (n, n), 1)
    square = jnp.where(row <= col, gram[0], gram[1])
    diag = jnp.diagonal(gram[1])[None, :]
    pad = jnp.zeros((7, n), gram.dtype)
    return jnp.concatenate([square, diag, pad], axis=0)


def unpack_pair(packed):
    n = packed.shape[-1]
    square = packed[:n]
    diag = packed[n]
    row = lax.broadcasted_iota(jnp.int32, (n, n), 0)
    col = lax.broadcasted_iota(jnp.int32, (n, n), 1)
    flipped = square.T
    first = jnp.where(row <= col, square, flipped)
    second = jnp.where(row > col, square, jnp.where(row < col, flipped, jnp.diag(diag)))
    return jnp.stack([first, second])


def chol_inv_kernel(g_ref, rt_ref, x_ref, s_ref):
    planes, n, _ = g_ref.shape
    s_ref[...] = g_ref[...]
    rr = lax.broadcasted_iota(jnp.int32, (n, n), 0)
    cc = lax.broadcasted_iota(jnp.int32, (n, n), 1)
    eye = jnp.where(rr == cc, 1.0, 0.0).astype(jnp.float32)
    for p in range(planes):
        x_ref[p] = eye
    rt_ref[...] = jnp.zeros(rt_ref.shape, jnp.float32)
    lane = lax.broadcasted_iota(jnp.int32, (1, n), 1)
    for j in range(n):
        lo = (j // 8) * 8
        rows = lax.broadcasted_iota(jnp.int32, (n - lo, 1), 0) + lo
        for p in range(planes):
            rowj = s_ref[p, j:j + 1, :]
            root = jnp.sqrt(rowj[:, j:j + 1])
            inv = 1.0 / root
            lrow = jnp.where(lane > j, rowj * inv, jnp.where(lane == j, root, 0.0))
            rt_ref[p, j:j + 1, :] = lrow
            blk = s_ref[p, lo:, :]
            lcol = jnp.where(rows > j, blk[:, j:j + 1] * inv, 0.0)
            s_ref[p, lo:, :] = blk - lcol * lrow
            xrow = x_ref[p, j:j + 1, :] * inv
            xblk = x_ref[p, lo:, :]
            x_ref[p, lo:, :] = jnp.where(rows == j, xrow, xblk - lcol * xrow)

def chol_inv(gram):
    planes, n, _ = gram.shape
    return pl.pallas_call(
        chol_inv_kernel,
        out_shape=(jax.ShapeDtypeStruct(gram.shape, jnp.float32),) * 2,
        in_specs=[pl.BlockSpec(memory_space=pltpu.VMEM)],
        out_specs=(pl.BlockSpec(memory_space=pltpu.VMEM),) * 2,
        scratch_shapes=[pltpu.VMEM(gram.shape, jnp.float32)],
    )(gram)


def local(u_field, w_field):
    planes, rows_x, rows_z, snaps = u_field.shape
    padded_u = with_halo(u_field, (("gz", 2),), 2).astype(jnp.float32)
    padded_w = with_halo(w_field, (("gx", 1),), 2).astype(jnp.float32)
    span_diff = 8.0 * (padded_u[:, :, 3:-1] - padded_u[:, :, 1:-3]) - (
        padded_u[:, :, 4:] - padded_u[:, :, :-4]
    )
    stream_diff = 8.0 * (padded_w[:, 3:-1] - padded_w[:, 1:-3]) - (
        padded_w[:, 4:] - padded_w[:, :-4]
    )
    vorticity = span_diff / (12.0 * span_step) - stream_diff / 12.0
    columns = vorticity.reshape(planes, rows_x * rows_z, snaps)
    gram_local = jnp.einsum(
        "pcs,pct->pst",
        columns,
        columns,
        precision=lax.Precision.HIGHEST,
        preferred_element_type=jnp.float32,
    )
    if planes == 2:
        gram_sum = unpack_pair(butterfly_sum(pack_pair(gram_local), ("gx", "gz")))
    else:
        gram_sum = butterfly_sum(gram_local, ("gx", "gz"))
    total_cells = rows_x * rows_z * lax.axis_size("gz") * lax.axis_size("gx")
    gram = gram_sum / total_cells
    factor_r, lower_inverse = chol_inv(gram)
    modes = jnp.einsum(
        "pcs,pts->pct",
        columns,
        lower_inverse,
        precision=lax.Precision.HIGHEST,
        preferred_element_type=jnp.float32,
    )
    modes = modes.reshape(planes, rows_x, rows_z, snaps)
    return (modes, factor_r)


def solution(mesh):
    return jax.shard_map(
        local,
        mesh=mesh,
        in_specs=(P(None, "gx", "gz", None), P(None, "gx", "gz", None)),
        out_specs=(P(None, "gx", "gz", None), P()),
        check_vma=False,
    )
```

```python
import jax
import jax.numpy as jnp
from jax import lax
from jax.experimental import pallas as pl
from jax.experimental.pallas import tpu as pltpu
from jax.sharding import PartitionSpec as P

span_step = 0.75


def with_halo(cells, sides, width):
    for axis, dim in sides:
        count = lax.axis_size(axis)
        head = lax.slice_in_dim(cells, 0, width, axis=dim)
        tail = lax.slice_in_dim(cells, cells.shape[dim] - width, cells.shape[dim], axis=dim)
        cells = jnp.concatenate(
            [
                lax.ppermute(tail, axis, [(i, (i + 1) % count) for i in range(count)]),
                cells,
                lax.ppermute(head, axis, [((i + 1) % count, i) for i in range(count)]),
            ],
            axis=dim,
        )
    return cells


def butterfly_sum(x, axes):
    for axis in axes:
        count = lax.axis_size(axis)
        step = 1
        while step < count:
            x = x + lax.ppermute(x, axis, [(i, i ^ step) for i in range(count)])
            step *= 2
    return x


def split_gram(columns):
    head32 = lax.reduce_precision(columns, exponent_bits=8, mantissa_bits=7)
    head = head32.astype(jnp.bfloat16)
    tail = (columns - head32).astype(jnp.bfloat16)

    def dot(a, b):
        return jnp.einsum("pcs,pct->pst", a, b, preferred_element_type=jnp.float32)

    cross = dot(head, tail)
    return dot(head, head) + (cross + jnp.swapaxes(cross, 1, 2)) + dot(tail, tail)


def pack_pair(gram):
    n = gram.shape[-1]
    row = lax.broadcasted_iota(jnp.int32, (n, n), 0)
    col = lax.broadcasted_iota(jnp.int32, (n, n), 1)
    square = jnp.where(row <= col, gram[0], gram[1])
    diag = jnp.sum(jnp.where(row == col, gram[1], 0.0), axis=0, keepdims=True)
    pad = jnp.zeros((7, n), gram.dtype)
    return jnp.concatenate([square, diag, pad], axis=0)


def unpack_pair(packed):
    n = packed.shape[-1]
    square = packed[:n]
    diag = packed[n]
    row = lax.broadcasted_iota(jnp.int32, (n, n), 0)
    col = lax.broadcasted_iota(jnp.int32, (n, n), 1)
    flipped = square.T
    first = jnp.where(row <= col, square, flipped)
    second = jnp.where(row > col, square, jnp.where(row < col, flipped, jnp.diag(diag)))
    return jnp.stack([first, second])


def chol_inv_kernel(g_ref, rt_ref, x_ref, s_ref):
    planes, n, _ = g_ref.shape
    s_ref[...] = g_ref[...]
    rr = lax.broadcasted_iota(jnp.int32, (n, n), 0)
    cc = lax.broadcasted_iota(jnp.int32, (n, n), 1)
    eye = jnp.where(rr == cc, 1.0, 0.0).astype(jnp.float32)
    for p in range(planes):
        x_ref[p] = eye
    rt_ref[...] = jnp.zeros(rt_ref.shape, jnp.float32)
    lane = lax.broadcasted_iota(jnp.int32, (1, n), 1)
    for j in range(n):
        lo = (j // 8) * 8
        rows = lax.broadcasted_iota(jnp.int32, (n - lo, 1), 0) + lo
        for p in range(planes):
            rowj = s_ref[p, j:j + 1, :]
            root = jnp.sqrt(rowj[:, j:j + 1])
            inv = 1.0 / root
            lrow = jnp.where(lane > j, rowj * inv, jnp.where(lane == j, root, 0.0))
            rt_ref[p, j:j + 1, :] = lrow
            blk = s_ref[p, lo:, :]
            lcol = jnp.where(rows > j, blk[:, j:j + 1] * inv, 0.0)
            s_ref[p, lo:, :] = blk - lcol * lrow
            xrow = x_ref[p, j:j + 1, :] * inv
            xblk = x_ref[p, lo:, :]
            x_ref[p, lo:, :] = jnp.where(rows == j, xrow, xblk - lcol * xrow)

def chol_inv(gram):
    planes, n, _ = gram.shape
    return pl.pallas_call(
        chol_inv_kernel,
        out_shape=(jax.ShapeDtypeStruct(gram.shape, jnp.float32),) * 2,
        in_specs=[pl.BlockSpec(memory_space=pltpu.VMEM)],
        out_specs=(pl.BlockSpec(memory_space=pltpu.VMEM),) * 2,
        scratch_shapes=[pltpu.VMEM(gram.shape, jnp.float32)],
    )(gram)


def local(u_field, w_field):
    planes, rows_x, rows_z, snaps = u_field.shape
    padded_u = with_halo(u_field, (("gz", 2),), 2).astype(jnp.float32)
    padded_w = with_halo(w_field, (("gx", 1),), 2).astype(jnp.float32)
    span_diff = 8.0 * (padded_u[:, :, 3:-1] - padded_u[:, :, 1:-3]) - (
        padded_u[:, :, 4:] - padded_u[:, :, :-4]
    )
    stream_diff = 8.0 * (padded_w[:, 3:-1] - padded_w[:, 1:-3]) - (
        padded_w[:, 4:] - padded_w[:, :-4]
    )
    vorticity = span_diff / (12.0 * span_step) - stream_diff / 12.0
    columns = vorticity.reshape(planes, rows_x * rows_z, snaps)
    gram_local = split_gram(columns)
    if planes == 2:
        gram_sum = unpack_pair(butterfly_sum(pack_pair(gram_local), ("gx", "gz")))
    else:
        gram_sum = butterfly_sum(gram_local, ("gx", "gz"))
    total_cells = rows_x * rows_z * lax.axis_size("gz") * lax.axis_size("gx")
    gram = gram_sum / total_cells
    factor_r, lower_inverse = chol_inv(gram)
    modes = jnp.einsum(
        "pcs,pts->pct",
        columns,
        lower_inverse,
        precision=lax.Precision.HIGH,
        preferred_element_type=jnp.float32,
    )
    modes = modes.reshape(planes, rows_x, rows_z, snaps)
    return (modes, factor_r)


def solution(mesh):
    return jax.shard_map(
        local,
        mesh=mesh,
        in_specs=(P(None, "gx", "gz", None), P(None, "gx", "gz", None)),
        out_specs=(P(None, "gx", "gz", None), P()),
        check_vma=False,
    )
```

```python
import jax
import jax.numpy as jnp
from jax import lax
from jax.experimental import pallas as pl
from jax.experimental.pallas import tpu as pltpu
from jax.sharding import PartitionSpec as P

span_step = 0.75


def with_halo(cells, sides, width):
    for axis, dim in sides:
        count = lax.axis_size(axis)
        head = lax.slice_in_dim(cells, 0, width, axis=dim)
        tail = lax.slice_in_dim(cells, cells.shape[dim] - width, cells.shape[dim], axis=dim)
        cells = jnp.concatenate(
            [
                lax.ppermute(tail, axis, [(i, (i + 1) % count) for i in range(count)]),
                cells,
                lax.ppermute(head, axis, [((i + 1) % count, i) for i in range(count)]),
            ],
            axis=dim,
        )
    return cells


def butterfly_sum(x, axes):
    for axis in axes:
        count = lax.axis_size(axis)
        step = 1
        while step < count:
            x = x + lax.ppermute(x, axis, [(i, i ^ step) for i in range(count)])
            step *= 2
    return x


def split_gram(columns):
    head32 = lax.reduce_precision(columns, exponent_bits=8, mantissa_bits=7)
    head = head32.astype(jnp.bfloat16)
    tail = (columns - head32).astype(jnp.bfloat16)

    def dot(a, b):
        return jnp.einsum("pcs,pct->pst", a, b, preferred_element_type=jnp.float32)

    cross = dot(head, tail)
    return dot(head, head) + (cross + jnp.swapaxes(cross, 1, 2)) + dot(tail, tail)


def chol_inv_kernel(g_ref, rt_ref, x_ref, s_ref):
    planes, n, _ = g_ref.shape
    s_ref[...] = g_ref[...]
    rr = lax.broadcasted_iota(jnp.int32, (n, n), 0)
    cc = lax.broadcasted_iota(jnp.int32, (n, n), 1)
    eye = jnp.where(rr == cc, 1.0, 0.0).astype(jnp.float32)
    for p in range(planes):
        x_ref[p] = eye
    lane = lax.broadcasted_iota(jnp.int32, (1, n), 1)
    pivot = [g_ref[p, 0:1, :] for p in range(planes)]
    for j in range(n):
        lo = (j // 8) * 8
        rows = lax.broadcasted_iota(jnp.int32, (n - lo, 1), 0) + lo
        for p in range(planes):
            rowj = pivot[p]
            root = jnp.sqrt(rowj[:, j:j + 1])
            inv = 1.0 / root
            lrow = jnp.where(lane > j, rowj * inv, jnp.where(lane == j, root, 0.0))
            rt_ref[p, j:j + 1, :] = lrow
            if j + 1 < n:
                nxt = s_ref[p, j + 1:j + 2, :]
                pivot[p] = nxt - (nxt[:, j:j + 1] * inv) * lrow
            blk = s_ref[p, lo:, :]
            lcol = jnp.where(rows > j, blk[:, j:j + 1] * inv, 0.0)
            s_ref[p, lo:, :] = blk - lcol * lrow
            xrow = x_ref[p, j:j + 1, :] * inv
            xblk = x_ref[p, lo:, :]
            x_ref[p, lo:, :] = jnp.where(rows == j, xrow, xblk - lcol * xrow)

def chol_inv(gram):
    planes, n, _ = gram.shape
    return pl.pallas_call(
        chol_inv_kernel,
        out_shape=(jax.ShapeDtypeStruct(gram.shape, jnp.float32),) * 2,
        in_specs=[pl.BlockSpec(memory_space=pltpu.VMEM)],
        out_specs=(pl.BlockSpec(memory_space=pltpu.VMEM),) * 2,
        scratch_shapes=[pltpu.VMEM(gram.shape, jnp.float32)],
    )(gram)


def vorticity_of(padded_u, padded_w):
    padded_u = padded_u.astype(jnp.float32)
    padded_w = padded_w.astype(jnp.float32)
    span_diff = 8.0 * (padded_u[:, :, 3:-1] - padded_u[:, :, 1:-3]) - (
        padded_u[:, :, 4:] - padded_u[:, :, :-4]
    )
    stream_diff = 8.0 * (padded_w[:, 3:-1] - padded_w[:, 1:-3]) - (
        padded_w[:, 4:] - padded_w[:, :-4]
    )
    vorticity = span_diff / (12.0 * span_step) - stream_diff / 12.0
    planes, rows_x, rows_z, snaps = vorticity.shape
    return vorticity.reshape(planes, rows_x * rows_z, snaps)


def symmetric(gram):
    n = gram.shape[-1]
    row = lax.broadcasted_iota(jnp.int32, (n, n), 0)
    col = lax.broadcasted_iota(jnp.int32, (n, n), 1)
    return jnp.where(row <= col, gram, jnp.swapaxes(gram, 1, 2))


def local(u_field, w_field):
    planes, rows_x, rows_z, snaps = u_field.shape
    padded_u = with_halo(u_field, (("gz", 2),), 2)
    padded_w = with_halo(w_field, (("gx", 1),), 2)
    total_cells = rows_x * rows_z * lax.axis_size("gz") * lax.axis_size("gx")
    modes, factor_r = [], []
    later_u, later_w = padded_u, padded_w
    for plane in range(planes):
        part = vorticity_of(later_u[plane:plane + 1], later_w[plane:plane + 1])
        gram_local = symmetric(split_gram(part))
        gram_local, later_u, later_w = lax.optimization_barrier((gram_local, later_u, later_w))
        gram = butterfly_sum(gram_local, ("gx", "gz")) / total_cells
        upper, lower_inverse = chol_inv(gram)
        factor_r.append(upper)
        modes.append(
            jnp.einsum(
                "pcs,pts->pct",
                part,
                lower_inverse,
                precision=lax.Precision.HIGH,
                preferred_element_type=jnp.float32,
            )
        )
    modes = jnp.concatenate(modes, axis=0).reshape(planes, rows_x, rows_z, snaps)
    factor_r = jnp.concatenate(factor_r, axis=0)
    return (modes, factor_r)

def solution(mesh):
    return jax.shard_map(
        local,
        mesh=mesh,
        in_specs=(P(None, "gx", "gz", None), P(None, "gx", "gz", None)),
        out_specs=(P(None, "gx", "gz", None), P()),
        check_vma=False,
    )
```

```python
import jax
import jax.numpy as jnp
from jax import lax
from jax.experimental import pallas as pl
from jax.experimental.pallas import tpu as pltpu
from jax.sharding import PartitionSpec as P

span_step = 0.75


def with_halo(cells, sides, width):
    for axis, dim in sides:
        count = lax.axis_size(axis)
        head = lax.slice_in_dim(cells, 0, width, axis=dim)
        tail = lax.slice_in_dim(cells, cells.shape[dim] - width, cells.shape[dim], axis=dim)
        cells = jnp.concatenate(
            [
                lax.ppermute(tail, axis, [(i, (i + 1) % count) for i in range(count)]),
                cells,
                lax.ppermute(head, axis, [((i + 1) % count, i) for i in range(count)]),
            ],
            axis=dim,
        )
    return cells


def butterfly_sum(x, axes):
    for axis in axes:
        count = lax.axis_size(axis)
        step = 1
        while step < count:
            x = x + lax.ppermute(x, axis, [(i, i ^ step) for i in range(count)])
            step *= 2
    return x


def split_gram(columns):
    head32 = lax.reduce_precision(columns, exponent_bits=8, mantissa_bits=7)
    head = head32.astype(jnp.bfloat16)
    tail = (columns - head32).astype(jnp.bfloat16)

    def dot(a, b):
        return jnp.einsum("pcs,pct->pst", a, b, preferred_element_type=jnp.float32)

    cross = dot(head, tail)
    return dot(head, head) + (cross + jnp.swapaxes(cross, 1, 2)) + dot(tail, tail)


def pack_pair(gram):
    n = gram.shape[-1]
    row = lax.broadcasted_iota(jnp.int32, (n, n), 0)
    col = lax.broadcasted_iota(jnp.int32, (n, n), 1)
    square = jnp.where(row <= col, gram[0], gram[1])
    diag = jnp.sum(jnp.where(row == col, gram[1], 0.0), axis=0, keepdims=True)
    pad = jnp.zeros((7, n), gram.dtype)
    return jnp.concatenate([square, diag, pad], axis=0)


def unpack_pair(packed):
    n = packed.shape[-1]
    square = packed[:n]
    diag = packed[n]
    row = lax.broadcasted_iota(jnp.int32, (n, n), 0)
    col = lax.broadcasted_iota(jnp.int32, (n, n), 1)
    flipped = square.T
    first = jnp.where(row <= col, square, flipped)
    second = jnp.where(row > col, square, jnp.where(row < col, flipped, jnp.diag(diag)))
    return jnp.stack([first, second])


def chol_inv_kernel(g_ref, rt_ref, x_ref, s_ref):
    planes, n, _ = g_ref.shape
    s_ref[...] = g_ref[...]
    rr = lax.broadcasted_iota(jnp.int32, (n, n), 0)
    cc = lax.broadcasted_iota(jnp.int32, (n, n), 1)
    eye = jnp.where(rr == cc, 1.0, 0.0).astype(jnp.float32)
    for p in range(planes):
        x_ref[p] = eye
    lane = lax.broadcasted_iota(jnp.int32, (1, n), 1)
    pivot = [g_ref[p, 0:1, :] for p in range(planes)]
    for j in range(n):
        lo = (j // 8) * 8
        rows = lax.broadcasted_iota(jnp.int32, (n - lo, 1), 0) + lo
        for p in range(planes):
            rowj = pivot[p]
            root = jnp.sqrt(rowj[:, j:j + 1])
            inv = lax.rsqrt(rowj[:, j:j + 1])
            lrow = jnp.where(lane > j, rowj * inv, jnp.where(lane == j, root, 0.0))
            rt_ref[p, j:j + 1, :] = lrow
            if j + 1 < n:
                nxt = s_ref[p, j + 1:j + 2, :]
                pivot[p] = nxt - (nxt[:, j:j + 1] * inv) * lrow
            blk = s_ref[p, lo:, :]
            lcol = jnp.where(rows > j, blk[:, j:j + 1] * inv, 0.0)
            s_ref[p, lo:, :] = blk - lcol * lrow
            xrow = x_ref[p, j:j + 1, :] * inv
            xblk = x_ref[p, lo:, :]
            x_ref[p, lo:, :] = jnp.where(rows == j, xrow, xblk - lcol * xrow)

def chol_inv(gram):
    planes, n, _ = gram.shape
    return pl.pallas_call(
        chol_inv_kernel,
        out_shape=(jax.ShapeDtypeStruct(gram.shape, jnp.float32),) * 2,
        in_specs=[pl.BlockSpec(memory_space=pltpu.VMEM)],
        out_specs=(pl.BlockSpec(memory_space=pltpu.VMEM),) * 2,
        scratch_shapes=[pltpu.VMEM(gram.shape, jnp.float32)],
    )(gram)


def local(u_field, w_field):
    planes, rows_x, rows_z, snaps = u_field.shape
    padded_u = with_halo(u_field, (("gz", 2),), 2).astype(jnp.float32)
    padded_w = with_halo(w_field, (("gx", 1),), 2).astype(jnp.float32)
    span_diff = 8.0 * (padded_u[:, :, 3:-1] - padded_u[:, :, 1:-3]) - (
        padded_u[:, :, 4:] - padded_u[:, :, :-4]
    )
    stream_diff = 8.0 * (padded_w[:, 3:-1] - padded_w[:, 1:-3]) - (
        padded_w[:, 4:] - padded_w[:, :-4]
    )
    vorticity = span_diff / (12.0 * span_step) - stream_diff / 12.0
    columns = vorticity.reshape(planes, rows_x * rows_z, snaps)
    gram_local = split_gram(columns)
    if planes == 2:
        gram_sum = unpack_pair(butterfly_sum(pack_pair(gram_local), ("gx", "gz")))
    else:
        gram_sum = butterfly_sum(gram_local, ("gx", "gz"))
    total_cells = rows_x * rows_z * lax.axis_size("gz") * lax.axis_size("gx")
    gram = gram_sum / total_cells
    factor_r, lower_inverse = chol_inv(gram)
    modes = jnp.einsum(
        "pcs,pts->pct",
        columns,
        lower_inverse,
        precision=lax.Precision.HIGH,
        preferred_element_type=jnp.float32,
    )
    modes = modes.reshape(planes, rows_x, rows_z, snaps)
    return (modes, factor_r)


def solution(mesh):
    return jax.shard_map(
        local,
        mesh=mesh,
        in_specs=(P(None, "gx", "gz", None), P(None, "gx", "gz", None)),
        out_specs=(P(None, "gx", "gz", None), P()),
        check_vma=False,
    )
```

```python
import jax
import jax.numpy as jnp
from jax import lax
from jax.experimental import pallas as pl
from jax.experimental.pallas import tpu as pltpu
from jax.sharding import PartitionSpec as P

span_step = 0.75


def with_halo(cells, sides, width):
    for axis, dim in sides:
        count = lax.axis_size(axis)
        head = lax.slice_in_dim(cells, 0, width, axis=dim)
        tail = lax.slice_in_dim(cells, cells.shape[dim] - width, cells.shape[dim], axis=dim)
        cells = jnp.concatenate(
            [
                lax.ppermute(tail, axis, [(i, (i + 1) % count) for i in range(count)]),
                cells,
                lax.ppermute(head, axis, [((i + 1) % count, i) for i in range(count)]),
            ],
            axis=dim,
        )
    return cells


def butterfly_sum(x, axes):
    for axis in axes:
        count = lax.axis_size(axis)
        step = 1
        while step < count:
            x = x + lax.ppermute(x, axis, [(i, i ^ step) for i in range(count)])
            step *= 2
    return x


def split(values):
    head32 = lax.reduce_precision(values, exponent_bits=8, mantissa_bits=7)
    return head32.astype(jnp.bfloat16), (values - head32).astype(jnp.bfloat16)


def split_gram(head, tail):
    def dot(a, b):
        return jnp.einsum("pcs,pct->pst", a, b, preferred_element_type=jnp.float32)

    cross = dot(head, tail)
    return dot(head, head) + (cross + jnp.swapaxes(cross, 1, 2)) + dot(tail, tail)


def split_modes(head, tail, lower_inverse):
    inv_head, inv_tail = split(lower_inverse)

    def dot(a, b):
        return jnp.einsum("pcs,pts->pct", a, b, preferred_element_type=jnp.float32)

    return dot(head, inv_head) + (dot(head, inv_tail) + dot(tail, inv_head))

def pack_pair(gram):
    n = gram.shape[-1]
    row = lax.broadcasted_iota(jnp.int32, (n, n), 0)
    col = lax.broadcasted_iota(jnp.int32, (n, n), 1)
    square = jnp.where(row <= col, gram[0], gram[1])
    diag = jnp.sum(jnp.where(row == col, gram[1], 0.0), axis=0, keepdims=True)
    pad = jnp.zeros((7, n), gram.dtype)
    return jnp.concatenate([square, diag, pad], axis=0)


def unpack_pair(packed):
    n = packed.shape[-1]
    square = packed[:n]
    diag = packed[n]
    row = lax.broadcasted_iota(jnp.int32, (n, n), 0)
    col = lax.broadcasted_iota(jnp.int32, (n, n), 1)
    flipped = square.T
    first = jnp.where(row <= col, square, flipped)
    second = jnp.where(row > col, square, jnp.where(row < col, flipped, jnp.diag(diag)))
    return jnp.stack([first, second])


def chol_inv_kernel(g_ref, rt_ref, x_ref, s_ref):
    planes, n, _ = g_ref.shape
    s_ref[...] = g_ref[...]
    rr = lax.broadcasted_iota(jnp.int32, (n, n), 0)
    cc = lax.broadcasted_iota(jnp.int32, (n, n), 1)
    eye = jnp.where(rr == cc, 1.0, 0.0).astype(jnp.float32)
    for p in range(planes):
        x_ref[p] = eye
    lane = lax.broadcasted_iota(jnp.int32, (1, n), 1)
    pivot = [g_ref[p, 0:1, :] for p in range(planes)]
    for j in range(n):
        lo = (j // 8) * 8
        rows = lax.broadcasted_iota(jnp.int32, (n - lo, 1), 0) + lo
        for p in range(planes):
            rowj = pivot[p]
            root = jnp.sqrt(rowj[:, j:j + 1])
            inv = lax.rsqrt(rowj[:, j:j + 1])
            lrow = jnp.where(lane > j, rowj * inv, jnp.where(lane == j, root, 0.0))
            rt_ref[p, j:j + 1, :] = lrow
            if j + 1 < n:
                nxt = s_ref[p, j + 1:j + 2, :]
                pivot[p] = nxt - (nxt[:, j:j + 1] * inv) * lrow
            blk = s_ref[p, lo:, :]
            lcol = jnp.where(rows > j, blk[:, j:j + 1] * inv, 0.0)
            s_ref[p, lo:, :] = blk - lcol * lrow
            xrow = x_ref[p, j:j + 1, :] * inv
            xblk = x_ref[p, lo:, :]
            x_ref[p, lo:, :] = jnp.where(rows == j, xrow, xblk - lcol * xrow)

def chol_inv(gram):
    planes, n, _ = gram.shape
    return pl.pallas_call(
        chol_inv_kernel,
        out_shape=(jax.ShapeDtypeStruct(gram.shape, jnp.float32),) * 2,
        in_specs=[pl.BlockSpec(memory_space=pltpu.VMEM)],
        out_specs=(pl.BlockSpec(memory_space=pltpu.VMEM),) * 2,
        scratch_shapes=[pltpu.VMEM(gram.shape, jnp.float32)],
    )(gram)


def local(u_field, w_field):
    planes, rows_x, rows_z, snaps = u_field.shape
    padded_u = with_halo(u_field, (("gz", 2),), 2).astype(jnp.float32)
    padded_w = with_halo(w_field, (("gx", 1),), 2).astype(jnp.float32)
    span_diff = 8.0 * (padded_u[:, :, 3:-1] - padded_u[:, :, 1:-3]) - (
        padded_u[:, :, 4:] - padded_u[:, :, :-4]
    )
    stream_diff = 8.0 * (padded_w[:, 3:-1] - padded_w[:, 1:-3]) - (
        padded_w[:, 4:] - padded_w[:, :-4]
    )
    vorticity = span_diff / (12.0 * span_step) - stream_diff / 12.0
    columns = vorticity.reshape(planes, rows_x * rows_z, snaps)
    head, tail = lax.optimization_barrier(split(columns))
    gram_local = split_gram(head, tail)
    if planes == 2:
        gram_sum = unpack_pair(butterfly_sum(pack_pair(gram_local), ("gx", "gz")))
    else:
        gram_sum = butterfly_sum(gram_local, ("gx", "gz"))
    total_cells = rows_x * rows_z * lax.axis_size("gz") * lax.axis_size("gx")
    gram = gram_sum / total_cells
    factor_r, lower_inverse = chol_inv(gram)
    modes = split_modes(head, tail, lower_inverse)
    modes = modes.reshape(planes, rows_x, rows_z, snaps)
    return (modes, factor_r)


def solution(mesh):
    return jax.shard_map(
        local,
        mesh=mesh,
        in_specs=(P(None, "gx", "gz", None), P(None, "gx", "gz", None)),
        out_specs=(P(None, "gx", "gz", None), P()),
        check_vma=False,
    )
```

```python
import jax
import jax.numpy as jnp
from jax import lax
from jax.experimental import pallas as pl
from jax.experimental.pallas import tpu as pltpu
from jax.sharding import PartitionSpec as P

span_step = 0.75


def with_halo(cells, sides, width):
    for axis, dim in sides:
        count = lax.axis_size(axis)
        head = lax.slice_in_dim(cells, 0, width, axis=dim)
        tail = lax.slice_in_dim(cells, cells.shape[dim] - width, cells.shape[dim], axis=dim)
        cells = jnp.concatenate(
            [
                lax.ppermute(tail, axis, [(i, (i + 1) % count) for i in range(count)]),
                cells,
                lax.ppermute(head, axis, [((i + 1) % count, i) for i in range(count)]),
            ],
            axis=dim,
        )
    return cells


def butterfly_sum(x, axes):
    for axis in axes:
        count = lax.axis_size(axis)
        step = 1
        while step < count:
            x = x + lax.ppermute(x, axis, [(i, i ^ step) for i in range(count)])
            step *= 2
    return x


def split(values):
    head32 = lax.reduce_precision(values, exponent_bits=8, mantissa_bits=7)
    return head32.astype(jnp.bfloat16), (values - head32).astype(jnp.bfloat16)


def split_gram(head, tail):
    def dot(a, b):
        return jnp.einsum("pcs,pct->pst", a, b, preferred_element_type=jnp.float32)

    cross = dot(head, tail)
    return dot(head, head) + (cross + jnp.swapaxes(cross, 1, 2)) + dot(tail, tail)


def split_modes(stacked, lower_inverse):
    inv_head, inv_tail = split(lower_inverse)
    weights = jnp.concatenate([inv_head, inv_head, inv_tail], axis=2)
    return jnp.einsum("pcs,pts->pct", stacked, weights, preferred_element_type=jnp.float32)

def pack_pair(gram):
    n = gram.shape[-1]
    row = lax.broadcasted_iota(jnp.int32, (n, n), 0)
    col = lax.broadcasted_iota(jnp.int32, (n, n), 1)
    square = jnp.where(row <= col, gram[0], gram[1])
    diag = jnp.sum(jnp.where(row == col, gram[1], 0.0), axis=0, keepdims=True)
    pad = jnp.zeros((7, n), gram.dtype)
    return jnp.concatenate([square, diag, pad], axis=0)


def unpack_pair(packed):
    n = packed.shape[-1]
    square = packed[:n]
    diag = packed[n]
    row = lax.broadcasted_iota(jnp.int32, (n, n), 0)
    col = lax.broadcasted_iota(jnp.int32, (n, n), 1)
    flipped = square.T
    first = jnp.where(row <= col, square, flipped)
    second = jnp.where(row > col, square, jnp.where(row < col, flipped, jnp.diag(diag)))
    return jnp.stack([first, second])


def chol_inv_kernel(g_ref, rt_ref, x_ref, s_ref):
    planes, n, _ = g_ref.shape
    s_ref[...] = g_ref[...]
    rr = lax.broadcasted_iota(jnp.int32, (n, n), 0)
    cc = lax.broadcasted_iota(jnp.int32, (n, n), 1)
    eye = jnp.where(rr == cc, 1.0, 0.0).astype(jnp.float32)
    for p in range(planes):
        x_ref[p] = eye
    lane = lax.broadcasted_iota(jnp.int32, (1, n), 1)
    pivot = [g_ref[p, 0:1, :] for p in range(planes)]
    for j in range(n):
        lo = (j // 8) * 8
        rows = lax.broadcasted_iota(jnp.int32, (n - lo, 1), 0) + lo
        for p in range(planes):
            rowj = pivot[p]
            root = jnp.sqrt(rowj[:, j:j + 1])
            inv = lax.rsqrt(rowj[:, j:j + 1])
            lrow = jnp.where(lane > j, rowj * inv, jnp.where(lane == j, root, 0.0))
            rt_ref[p, j:j + 1, :] = lrow
            if j + 1 < n:
                nxt = s_ref[p, j + 1:j + 2, :]
                pivot[p] = nxt - (nxt[:, j:j + 1] * inv) * lrow
            blk = s_ref[p, lo:, :]
            lcol = jnp.where(rows > j, blk[:, j:j + 1] * inv, 0.0)
            s_ref[p, lo:, :] = blk - lcol * lrow
            xrow = x_ref[p, j:j + 1, :] * inv
            xblk = x_ref[p, lo:, :]
            x_ref[p, lo:, :] = jnp.where(rows == j, xrow, xblk - lcol * xrow)

def chol_inv(gram):
    planes, n, _ = gram.shape
    return pl.pallas_call(
        chol_inv_kernel,
        out_shape=(jax.ShapeDtypeStruct(gram.shape, jnp.float32),) * 2,
        in_specs=[pl.BlockSpec(memory_space=pltpu.VMEM)],
        out_specs=(pl.BlockSpec(memory_space=pltpu.VMEM),) * 2,
        scratch_shapes=[pltpu.VMEM(gram.shape, jnp.float32)],
    )(gram)


def local(u_field, w_field):
    planes, rows_x, rows_z, snaps = u_field.shape
    padded_u = with_halo(u_field, (("gz", 2),), 2).astype(jnp.float32)
    padded_w = with_halo(w_field, (("gx", 1),), 2).astype(jnp.float32)
    span_diff = 8.0 * (padded_u[:, :, 3:-1] - padded_u[:, :, 1:-3]) - (
        padded_u[:, :, 4:] - padded_u[:, :, :-4]
    )
    stream_diff = 8.0 * (padded_w[:, 3:-1] - padded_w[:, 1:-3]) - (
        padded_w[:, 4:] - padded_w[:, :-4]
    )
    vorticity = span_diff / (12.0 * span_step) - stream_diff / 12.0
    columns = vorticity.reshape(planes, rows_x * rows_z, snaps)
    head, tail = split(columns)
    stacked = lax.optimization_barrier(jnp.concatenate([head, tail, head], axis=2))
    gram_local = split_gram(stacked[..., :snaps], stacked[..., snaps:2 * snaps])
    if planes == 2:
        gram_sum = unpack_pair(butterfly_sum(pack_pair(gram_local), ("gx", "gz")))
    else:
        gram_sum = butterfly_sum(gram_local, ("gx", "gz"))
    total_cells = rows_x * rows_z * lax.axis_size("gz") * lax.axis_size("gx")
    gram = gram_sum / total_cells
    factor_r, lower_inverse = chol_inv(gram)
    modes = split_modes(stacked, lower_inverse)
    modes = modes.reshape(planes, rows_x, rows_z, snaps)
    return (modes, factor_r)


def solution(mesh):
    return jax.shard_map(
        local,
        mesh=mesh,
        in_specs=(P(None, "gx", "gz", None), P(None, "gx", "gz", None)),
        out_specs=(P(None, "gx", "gz", None), P()),
        check_vma=False,
    )
```

```python
import jax
import jax.numpy as jnp
from jax import lax
from jax.experimental import pallas as pl
from jax.experimental.pallas import tpu as pltpu
from jax.sharding import PartitionSpec as P

span_step = 0.75


def with_halo(cells, sides, width):
    for axis, dim in sides:
        count = lax.axis_size(axis)
        head = lax.slice_in_dim(cells, 0, width, axis=dim)
        tail = lax.slice_in_dim(cells, cells.shape[dim] - width, cells.shape[dim], axis=dim)
        cells = jnp.concatenate(
            [
                lax.ppermute(tail, axis, [(i, (i + 1) % count) for i in range(count)]),
                cells,
                lax.ppermute(head, axis, [((i + 1) % count, i) for i in range(count)]),
            ],
            axis=dim,
        )
    return cells


def butterfly_sum(x, axes):
    for axis in axes:
        count = lax.axis_size(axis)
        step = 1
        while step < count:
            x = x + lax.ppermute(x, axis, [(i, i ^ step) for i in range(count)])
            step *= 2
    return x


def split(values):
    head32 = lax.reduce_precision(values, exponent_bits=8, mantissa_bits=7)
    return head32.astype(jnp.bfloat16), (values - head32).astype(jnp.bfloat16)


def split_gram(head, tail):
    def dot(a, b):
        return jnp.einsum("pcs,pct->pst", a, b, preferred_element_type=jnp.float32)

    cross = dot(head, tail)
    return dot(head, head) + (cross + jnp.swapaxes(cross, 1, 2)) + dot(tail, tail)


def split_modes(head, tail, lower_inverse):
    inv_head, inv_tail = split(lower_inverse)

    def dot(a, b):
        return jnp.einsum("pcs,pts->pct", a, b, preferred_element_type=jnp.float32)

    return dot(head, inv_head) + (dot(head, inv_tail) + dot(tail, inv_head))

def pack_pair(gram):
    n = gram.shape[-1]
    row = lax.broadcasted_iota(jnp.int32, (n, n), 0)
    col = lax.broadcasted_iota(jnp.int32, (n, n), 1)
    square = jnp.where(row <= col, gram[0], gram[1])
    diag = jnp.sum(jnp.where(row == col, gram[1], 0.0), axis=0, keepdims=True)
    pad = jnp.zeros((7, n), gram.dtype)
    return jnp.concatenate([square, diag, pad], axis=0)


def unpack_pair(packed):
    n = packed.shape[-1]
    square = packed[:n]
    diag = packed[n]
    row = lax.broadcasted_iota(jnp.int32, (n, n), 0)
    col = lax.broadcasted_iota(jnp.int32, (n, n), 1)
    flipped = square.T
    first = jnp.where(row <= col, square, flipped)
    second = jnp.where(row > col, square, jnp.where(row < col, flipped, jnp.diag(diag)))
    return jnp.stack([first, second])


def chol_inv_kernel(g_ref, rt_ref, x_ref, s_ref):
    planes, n, _ = g_ref.shape
    s_ref[...] = g_ref[...]
    rr = lax.broadcasted_iota(jnp.int32, (n, n), 0)
    cc = lax.broadcasted_iota(jnp.int32, (n, n), 1)
    eye = jnp.where(rr == cc, 1.0, 0.0).astype(jnp.float32)
    for p in range(planes):
        x_ref[p] = eye
    lane = lax.broadcasted_iota(jnp.int32, (1, n), 1)
    pivot = [g_ref[p, 0:1, :] for p in range(planes)]
    for j in range(n):
        lo = (j // 8) * 8
        rows = lax.broadcasted_iota(jnp.int32, (n - lo, 1), 0) + lo
        for p in range(planes):
            rowj = pivot[p]
            root = jnp.sqrt(rowj[:, j:j + 1])
            inv = lax.rsqrt(rowj[:, j:j + 1])
            lrow = rowj * inv
            rt_ref[p, j:j + 1, :] = jnp.where(lane > j, lrow, jnp.where(lane == j, root, 0.0))
            if j + 1 < n:
                nxt = s_ref[p, j + 1:j + 2, :]
                pivot[p] = nxt - (nxt[:, j:j + 1] * inv) * lrow
            blk = s_ref[p, lo:, :]
            lcol = jnp.where(rows > j, blk[:, j:j + 1] * inv, 0.0)
            s_ref[p, lo:, :] = blk - lcol * lrow
            xrow = x_ref[p, j:j + 1, :] * inv
            xblk = x_ref[p, lo:, :]
            x_ref[p, lo:, :] = jnp.where(rows == j, xrow, xblk - lcol * xrow)

def chol_inv(gram):
    planes, n, _ = gram.shape
    return pl.pallas_call(
        chol_inv_kernel,
        out_shape=(jax.ShapeDtypeStruct(gram.shape, jnp.float32),) * 2,
        in_specs=[pl.BlockSpec(memory_space=pltpu.VMEM)],
        out_specs=(pl.BlockSpec(memory_space=pltpu.VMEM),) * 2,
        scratch_shapes=[pltpu.VMEM(gram.shape, jnp.float32)],
    )(gram)


def local(u_field, w_field):
    planes, rows_x, rows_z, snaps = u_field.shape
    padded_u = with_halo(u_field, (("gz", 2),), 2).astype(jnp.float32)
    padded_w = with_halo(w_field, (("gx", 1),), 2).astype(jnp.float32)
    span_diff = 8.0 * (padded_u[:, :, 3:-1] - padded_u[:, :, 1:-3]) - (
        padded_u[:, :, 4:] - padded_u[:, :, :-4]
    )
    stream_diff = 8.0 * (padded_w[:, 3:-1] - padded_w[:, 1:-3]) - (
        padded_w[:, 4:] - padded_w[:, :-4]
    )
    vorticity = span_diff / (12.0 * span_step) - stream_diff / 12.0
    columns = vorticity.reshape(planes, rows_x * rows_z, snaps)
    head, tail = lax.optimization_barrier(split(columns))
    gram_local = split_gram(head, tail)
    if planes == 2:
        gram_sum = unpack_pair(butterfly_sum(pack_pair(gram_local), ("gx", "gz")))
    else:
        gram_sum = butterfly_sum(gram_local, ("gx", "gz"))
    total_cells = rows_x * rows_z * lax.axis_size("gz") * lax.axis_size("gx")
    gram = gram_sum / total_cells
    factor_r, lower_inverse = chol_inv(gram)
    modes = split_modes(head, tail, lower_inverse)
    modes = modes.reshape(planes, rows_x, rows_z, snaps)
    return (modes, factor_r)


def solution(mesh):
    return jax.shard_map(
        local,
        mesh=mesh,
        in_specs=(P(None, "gx", "gz", None), P(None, "gx", "gz", None)),
        out_specs=(P(None, "gx", "gz", None), P()),
        check_vma=False,
    )
```

```python
import jax
import jax.numpy as jnp
from jax import lax
from jax.experimental import pallas as pl
from jax.experimental.pallas import tpu as pltpu
from jax.sharding import PartitionSpec as P

span_step = 0.75


def with_halo(cells, sides, width):
    for axis, dim in sides:
        count = lax.axis_size(axis)
        head = lax.slice_in_dim(cells, 0, width, axis=dim)
        tail = lax.slice_in_dim(cells, cells.shape[dim] - width, cells.shape[dim], axis=dim)
        cells = jnp.concatenate(
            [
                lax.ppermute(tail, axis, [(i, (i + 1) % count) for i in range(count)]),
                cells,
                lax.ppermute(head, axis, [((i + 1) % count, i) for i in range(count)]),
            ],
            axis=dim,
        )
    return cells


def ring_stages(size):
    stages, step = [], 1
    while step < size:
        if step * 2 == size and size > 2:
            stages.append([size - 1 - p for p in range(size)])
        else:
            stages.append([p ^ step for p in range(size)])
        step *= 2
    return stages


def axis_stages(count, inner):
    if count % inner:
        inner = count
    outer = count // inner
    stages = [[i - i % inner + perm[i % inner] for i in range(count)] for perm in ring_stages(inner)]
    stages += [[perm[i // inner] * inner + i % inner for i in range(count)] for perm in ring_stages(outer)]
    return stages


def butterfly_sum(x, axes):
    for axis, inner in axes:
        count = lax.axis_size(axis)
        for partner in axis_stages(count, inner):
            x = x + lax.ppermute(x, axis, [(i, partner[i]) for i in range(count)])
    return x

def split(values):
    head32 = lax.reduce_precision(values, exponent_bits=8, mantissa_bits=7)
    return head32.astype(jnp.bfloat16), (values - head32).astype(jnp.bfloat16)


def split_gram(head, tail):
    def dot(a, b):
        return jnp.einsum("pcs,pct->pst", a, b, preferred_element_type=jnp.float32)

    cross = dot(head, tail)
    return dot(head, head) + (cross + jnp.swapaxes(cross, 1, 2)) + dot(tail, tail)


def split_modes(head, tail, lower_inverse):
    inv_head, inv_tail = split(lower_inverse)

    def dot(a, b):
        return jnp.einsum("pcs,pts->pct", a, b, preferred_element_type=jnp.float32)

    return dot(head, inv_head) + (dot(head, inv_tail) + dot(tail, inv_head))

def pack_pair(gram):
    n = gram.shape[-1]
    row = lax.broadcasted_iota(jnp.int32, (n, n), 0)
    col = lax.broadcasted_iota(jnp.int32, (n, n), 1)
    square = jnp.where(row <= col, gram[0], gram[1])
    diag = jnp.sum(jnp.where(row == col, gram[1], 0.0), axis=0, keepdims=True)
    pad = jnp.zeros((7, n), gram.dtype)
    return jnp.concatenate([square, diag, pad], axis=0)


def unpack_pair(packed):
    n = packed.shape[-1]
    square = packed[:n]
    diag = packed[n]
    row = lax.broadcasted_iota(jnp.int32, (n, n), 0)
    col = lax.broadcasted_iota(jnp.int32, (n, n), 1)
    flipped = square.T
    first = jnp.where(row <= col, square, flipped)
    second = jnp.where(row > col, square, jnp.where(row < col, flipped, jnp.diag(diag)))
    return jnp.stack([first, second])


def chol_inv_kernel(g_ref, rt_ref, x_ref, s_ref):
    planes, n, _ = g_ref.shape
    s_ref[...] = g_ref[...]
    rr = lax.broadcasted_iota(jnp.int32, (n, n), 0)
    cc = lax.broadcasted_iota(jnp.int32, (n, n), 1)
    eye = jnp.where(rr == cc, 1.0, 0.0).astype(jnp.float32)
    for p in range(planes):
        x_ref[p] = eye
    lane = lax.broadcasted_iota(jnp.int32, (1, n), 1)
    pivot = [g_ref[p, 0:1, :] for p in range(planes)]
    for j in range(n):
        lo = (j // 8) * 8
        rows = lax.broadcasted_iota(jnp.int32, (n - lo, 1), 0) + lo
        for p in range(planes):
            rowj = pivot[p]
            root = jnp.sqrt(rowj[:, j:j + 1])
            inv = lax.rsqrt(rowj[:, j:j + 1])
            lrow = rowj * inv
            rt_ref[p, j:j + 1, :] = jnp.where(lane > j, lrow, jnp.where(lane == j, root, 0.0))
            if j + 1 < n:
                nxt = s_ref[p, j + 1:j + 2, :]
                pivot[p] = nxt - (nxt[:, j:j + 1] * inv) * lrow
            blk = s_ref[p, lo:, :]
            lcol = jnp.where(rows > j, blk[:, j:j + 1] * inv, 0.0)
            s_ref[p, lo:, :] = blk - lcol * lrow
            xrow = x_ref[p, j:j + 1, :] * inv
            xblk = x_ref[p, lo:, :]
            x_ref[p, lo:, :] = jnp.where(rows == j, xrow, xblk - lcol * xrow)

def chol_inv(gram):
    planes, n, _ = gram.shape
    return pl.pallas_call(
        chol_inv_kernel,
        out_shape=(jax.ShapeDtypeStruct(gram.shape, jnp.float32),) * 2,
        in_specs=[pl.BlockSpec(memory_space=pltpu.VMEM)],
        out_specs=(pl.BlockSpec(memory_space=pltpu.VMEM),) * 2,
        scratch_shapes=[pltpu.VMEM(gram.shape, jnp.float32)],
    )(gram)


def local(u_field, w_field):
    planes, rows_x, rows_z, snaps = u_field.shape
    padded_u = with_halo(u_field, (("gz", 2),), 2).astype(jnp.float32)
    padded_w = with_halo(w_field, (("gx", 1),), 2).astype(jnp.float32)
    span_diff = 8.0 * (padded_u[:, :, 3:-1] - padded_u[:, :, 1:-3]) - (
        padded_u[:, :, 4:] - padded_u[:, :, :-4]
    )
    stream_diff = 8.0 * (padded_w[:, 3:-1] - padded_w[:, 1:-3]) - (
        padded_w[:, 4:] - padded_w[:, :-4]
    )
    vorticity = span_diff / (12.0 * span_step) - stream_diff / 12.0
    columns = vorticity.reshape(planes, rows_x * rows_z, snaps)
    head, tail = lax.optimization_barrier(split(columns))
    gram_local = split_gram(head, tail)
    if planes == 2:
        gram_sum = unpack_pair(butterfly_sum(pack_pair(gram_local), (("gx", 2), ("gz", 8))))
    else:
        gram_sum = butterfly_sum(gram_local, (("gx", 2), ("gz", 8)))
    total_cells = rows_x * rows_z * lax.axis_size("gz") * lax.axis_size("gx")
    gram = gram_sum / total_cells
    factor_r, lower_inverse = chol_inv(gram)
    modes = split_modes(head, tail, lower_inverse)
    modes = modes.reshape(planes, rows_x, rows_z, snaps)
    return (modes, factor_r)


def solution(mesh):
    return jax.shard_map(
        local,
        mesh=mesh,
        in_specs=(P(None, "gx", "gz", None), P(None, "gx", "gz", None)),
        out_specs=(P(None, "gx", "gz", None), P()),
        check_vma=False,
    )
```

```python
import jax
import jax.numpy as jnp
from jax import lax
from jax.experimental import pallas as pl
from jax.experimental.pallas import tpu as pltpu
from jax.sharding import PartitionSpec as P

span_step = 0.75


def with_halo(cells, sides, width):
    for axis, dim in sides:
        count = lax.axis_size(axis)
        head = lax.slice_in_dim(cells, 0, width, axis=dim)
        tail = lax.slice_in_dim(cells, cells.shape[dim] - width, cells.shape[dim], axis=dim)
        cells = jnp.concatenate(
            [
                lax.ppermute(tail, axis, [(i, (i + 1) % count) for i in range(count)]),
                cells,
                lax.ppermute(head, axis, [((i + 1) % count, i) for i in range(count)]),
            ],
            axis=dim,
        )
    return cells


def ring_stages(size):
    stages, step = [], 1
    while step < size:
        if step * 2 == size and size == 8:
            stages.append([6, 7, 4, 5, 2, 3, 0, 1])
        elif step * 2 == size and size > 2:
            stages.append([size - 1 - p for p in range(size)])
        else:
            stages.append([p ^ step for p in range(size)])
        step *= 2
    return stages


def axis_stages(count, inner):
    if count % inner:
        inner = count
    outer = count // inner
    stages = [[i - i % inner + perm[i % inner] for i in range(count)] for perm in ring_stages(inner)]
    stages += [[perm[i // inner] * inner + i % inner for i in range(count)] for perm in ring_stages(outer)]
    return stages


def butterfly_sum(x, axes):
    for axis, inner in axes:
        count = lax.axis_size(axis)
        for partner in axis_stages(count, inner):
            x = x + lax.ppermute(x, axis, [(i, partner[i]) for i in range(count)])
    return x

def split(values):
    head32 = lax.reduce_precision(values, exponent_bits=8, mantissa_bits=7)
    return head32.astype(jnp.bfloat16), (values - head32).astype(jnp.bfloat16)


def split_gram(head, tail):
    def dot(a, b):
        return jnp.einsum("pcs,pct->pst", a, b, preferred_element_type=jnp.float32)

    cross = dot(head, tail)
    return dot(head, head) + (cross + jnp.swapaxes(cross, 1, 2)) + dot(tail, tail)


def split_modes(head, tail, lower_inverse):
    inv_head, inv_tail = split(lower_inverse)

    def dot(a, b):
        return jnp.einsum("pcs,pts->pct", a, b, preferred_element_type=jnp.float32)

    return dot(head, inv_head) + (dot(head, inv_tail) + dot(tail, inv_head))

def pack_pair(gram):
    n = gram.shape[-1]
    row = lax.broadcasted_iota(jnp.int32, (n, n), 0)
    col = lax.broadcasted_iota(jnp.int32, (n, n), 1)
    square = jnp.where(row <= col, gram[0], gram[1])
    diag = jnp.sum(jnp.where(row == col, gram[1], 0.0), axis=0, keepdims=True)
    pad = jnp.zeros((7, n), gram.dtype)
    return jnp.concatenate([square, diag, pad], axis=0)


def unpack_pair(packed):
    n = packed.shape[-1]
    square = packed[:n]
    diag = packed[n]
    row = lax.broadcasted_iota(jnp.int32, (n, n), 0)
    col = lax.broadcasted_iota(jnp.int32, (n, n), 1)
    flipped = square.T
    first = jnp.where(row <= col, square, flipped)
    second = jnp.where(row > col, square, jnp.where(row < col, flipped, jnp.diag(diag)))
    return jnp.stack([first, second])


def chol_inv_kernel(g_ref, rt_ref, x_ref, s_ref):
    planes, n, _ = g_ref.shape
    s_ref[...] = g_ref[...]
    rr = lax.broadcasted_iota(jnp.int32, (n, n), 0)
    cc = lax.broadcasted_iota(jnp.int32, (n, n), 1)
    eye = jnp.where(rr == cc, 1.0, 0.0).astype(jnp.float32)
    for p in range(planes):
        x_ref[p] = eye
    lane = lax.broadcasted_iota(jnp.int32, (1, n), 1)
    pivot = [g_ref[p, 0:1, :] for p in range(planes)]
    for j in range(n):
        lo = (j // 8) * 8
        rows = lax.broadcasted_iota(jnp.int32, (n - lo, 1), 0) + lo
        for p in range(planes):
            rowj = pivot[p]
            root = jnp.sqrt(rowj[:, j:j + 1])
            inv = lax.rsqrt(rowj[:, j:j + 1])
            lrow = rowj * inv
            rt_ref[p, j:j + 1, :] = jnp.where(lane > j, lrow, jnp.where(lane == j, root, 0.0))
            if j + 1 < n:
                nxt = s_ref[p, j + 1:j + 2, :]
                pivot[p] = nxt - (nxt[:, j:j + 1] * inv) * lrow
            blk = s_ref[p, lo:, :]
            lcol = jnp.where(rows > j, blk[:, j:j + 1] * inv, 0.0)
            s_ref[p, lo:, :] = blk - lcol * lrow
            xrow = x_ref[p, j:j + 1, :] * inv
            xblk = x_ref[p, lo:, :]
            x_ref[p, lo:, :] = jnp.where(rows == j, xrow, xblk - lcol * xrow)

def chol_inv(gram):
    planes, n, _ = gram.shape
    return pl.pallas_call(
        chol_inv_kernel,
        out_shape=(jax.ShapeDtypeStruct(gram.shape, jnp.float32),) * 2,
        in_specs=[pl.BlockSpec(memory_space=pltpu.VMEM)],
        out_specs=(pl.BlockSpec(memory_space=pltpu.VMEM),) * 2,
        scratch_shapes=[pltpu.VMEM(gram.shape, jnp.float32)],
    )(gram)


def local(u_field, w_field):
    planes, rows_x, rows_z, snaps = u_field.shape
    padded_u = with_halo(u_field, (("gz", 2),), 2).astype(jnp.float32)
    padded_w = with_halo(w_field, (("gx", 1),), 2).astype(jnp.float32)
    span_diff = 8.0 * (padded_u[:, :, 3:-1] - padded_u[:, :, 1:-3]) - (
        padded_u[:, :, 4:] - padded_u[:, :, :-4]
    )
    stream_diff = 8.0 * (padded_w[:, 3:-1] - padded_w[:, 1:-3]) - (
        padded_w[:, 4:] - padded_w[:, :-4]
    )
    vorticity = span_diff / (12.0 * span_step) - stream_diff / 12.0
    columns = vorticity.reshape(planes, rows_x * rows_z, snaps)
    head, tail = lax.optimization_barrier(split(columns))
    gram_local = split_gram(head, tail)
    if planes == 2:
        gram_sum = unpack_pair(butterfly_sum(pack_pair(gram_local), (("gx", 2), ("gz", 8))))
    else:
        gram_sum = butterfly_sum(gram_local, (("gx", 2), ("gz", 8)))
    total_cells = rows_x * rows_z * lax.axis_size("gz") * lax.axis_size("gx")
    gram = gram_sum / total_cells
    factor_r, lower_inverse = chol_inv(gram)
    modes = split_modes(head, tail, lower_inverse)
    modes = modes.reshape(planes, rows_x, rows_z, snaps)
    return (modes, factor_r)


def solution(mesh):
    return jax.shard_map(
        local,
        mesh=mesh,
        in_specs=(P(None, "gx", "gz", None), P(None, "gx", "gz", None)),
        out_specs=(P(None, "gx", "gz", None), P()),
        check_vma=False,
    )
```

```python
import jax
import jax.numpy as jnp
from jax import lax
from jax.experimental import pallas as pl
from jax.experimental.pallas import tpu as pltpu
from jax.sharding import PartitionSpec as P

span_step = 0.75


def with_halo(cells, sides, width):
    for axis, dim in sides:
        count = lax.axis_size(axis)
        head = lax.slice_in_dim(cells, 0, width, axis=dim)
        tail = lax.slice_in_dim(cells, cells.shape[dim] - width, cells.shape[dim], axis=dim)
        cells = jnp.concatenate(
            [
                lax.ppermute(tail, axis, [(i, (i + 1) % count) for i in range(count)]),
                cells,
                lax.ppermute(head, axis, [((i + 1) % count, i) for i in range(count)]),
            ],
            axis=dim,
        )
    return cells


def ring_stages(size):
    stages, step = [], 1
    while step < size:
        if step * 2 == size and size == 8:
            stages.append([6, 7, 4, 5, 2, 3, 0, 1])
        elif step * 2 == size and size > 2:
            stages.append([size - 1 - p for p in range(size)])
        else:
            stages.append([p ^ step for p in range(size)])
        step *= 2
    return stages


def axis_stages(count, inner):
    if count % inner:
        inner = count
    outer = count // inner
    stages = [[i - i % inner + perm[i % inner] for i in range(count)] for perm in ring_stages(inner)]
    stages += [[perm[i // inner] * inner + i % inner for i in range(count)] for perm in ring_stages(outer)]
    return stages


def butterfly_sum(x, axes):
    for axis, inner in axes:
        count = lax.axis_size(axis)
        for partner in axis_stages(count, inner):
            x = x + lax.ppermute(x, axis, [(i, partner[i]) for i in range(count)])
    return x

def split(values):
    head32 = lax.reduce_precision(values, exponent_bits=8, mantissa_bits=7)
    return head32.astype(jnp.bfloat16), (values - head32).astype(jnp.bfloat16)


def split_gram(head, tail):
    def dot(a, b):
        return jnp.einsum("pcs,pct->pst", a, b, preferred_element_type=jnp.float32)

    cross = dot(head, tail)
    return dot(head, head) + (cross + jnp.swapaxes(cross, 1, 2)) + dot(tail, tail)


def split_modes(head, tail, lower_inverse):
    inv_head, inv_tail = split(lower_inverse)

    def dot(a, b):
        return jnp.einsum("pcs,pts->pct", a, b, preferred_element_type=jnp.float32)

    return dot(head, inv_head) + (dot(head, inv_tail) + dot(tail, inv_head))

def pack_pair(gram):
    n = gram.shape[-1]
    row = lax.broadcasted_iota(jnp.int32, (n, n), 0)
    col = lax.broadcasted_iota(jnp.int32, (n, n), 1)
    square = jnp.where(row <= col, gram[0], gram[1])
    diag = jnp.sum(jnp.where(row == col, gram[1], 0.0), axis=0, keepdims=True)
    pad = jnp.zeros((7, n), gram.dtype)
    return jnp.concatenate([square, diag, pad], axis=0)


def unpack_pair(packed):
    n = packed.shape[-1]
    square = packed[:n]
    diag = packed[n]
    row = lax.broadcasted_iota(jnp.int32, (n, n), 0)
    col = lax.broadcasted_iota(jnp.int32, (n, n), 1)
    flipped = square.T
    first = jnp.where(row <= col, square, flipped)
    second = jnp.where(row > col, square, jnp.where(row < col, flipped, jnp.diag(diag)))
    return jnp.stack([first, second])


def chol_inv_kernel(g_ref, rt_ref, x_ref, s_ref):
    planes, n, _ = g_ref.shape
    s_ref[...] = g_ref[...]
    rr = lax.broadcasted_iota(jnp.int32, (n, n), 0)
    cc = lax.broadcasted_iota(jnp.int32, (n, n), 1)
    eye = jnp.where(rr == cc, 1.0, 0.0).astype(jnp.float32)
    for p in range(planes):
        x_ref[p] = eye
    lane = lax.broadcasted_iota(jnp.int32, (1, n), 1)
    pivot = [g_ref[p, 0:1, :] for p in range(planes)]
    for j in range(n):
        lo = (j // 8) * 8
        rows = lax.broadcasted_iota(jnp.int32, (n - lo, 1), 0) + lo
        for p in range(planes):
            rowj = pivot[p]
            root = jnp.sqrt(rowj[:, j:j + 1])
            inv = lax.rsqrt(rowj[:, j:j + 1])
            lrow = rowj * inv
            rt_ref[p, j:j + 1, :] = jnp.where(lane > j, lrow, jnp.where(lane == j, root, 0.0))
            if j + 1 < n:
                nxt = s_ref[p, j + 1:j + 2, :]
                pivot[p] = nxt - (nxt[:, j:j + 1] * inv) * lrow
            blk = s_ref[p, lo:, :]
            lcol = jnp.where(rows > j, blk[:, j:j + 1] * inv, 0.0)
            s_ref[p, lo:, :] = blk - lcol * lrow
            xrow = x_ref[p, j:j + 1, :] * inv
            xblk = x_ref[p, lo:, :]
            x_ref[p, lo:, :] = jnp.where(rows == j, xrow, xblk - lcol * xrow)

def chol_inv(gram):
    planes, n, _ = gram.shape
    return pl.pallas_call(
        chol_inv_kernel,
        out_shape=(jax.ShapeDtypeStruct(gram.shape, jnp.float32),) * 2,
        in_specs=[pl.BlockSpec(memory_space=pltpu.VMEM)],
        out_specs=(pl.BlockSpec(memory_space=pltpu.VMEM),) * 2,
        scratch_shapes=[pltpu.VMEM(gram.shape, jnp.float32)],
        compiler_params=pltpu.CompilerParams(allow_input_fusion=[True]),
    )(gram)


def local(u_field, w_field):
    planes, rows_x, rows_z, snaps = u_field.shape
    padded_u = with_halo(u_field, (("gz", 2),), 2).astype(jnp.float32)
    padded_w = with_halo(w_field, (("gx", 1),), 2).astype(jnp.float32)
    span_diff = 8.0 * (padded_u[:, :, 3:-1] - padded_u[:, :, 1:-3]) - (
        padded_u[:, :, 4:] - padded_u[:, :, :-4]
    )
    stream_diff = 8.0 * (padded_w[:, 3:-1] - padded_w[:, 1:-3]) - (
        padded_w[:, 4:] - padded_w[:, :-4]
    )
    vorticity = span_diff / (12.0 * span_step) - stream_diff / 12.0
    columns = vorticity.reshape(planes, rows_x * rows_z, snaps)
    head, tail = lax.optimization_barrier(split(columns))
    gram_local = split_gram(head, tail)
    if planes == 2:
        gram_sum = unpack_pair(butterfly_sum(pack_pair(gram_local), (("gx", 2), ("gz", 8))))
    else:
        gram_sum = butterfly_sum(gram_local, (("gx", 2), ("gz", 8)))
    total_cells = rows_x * rows_z * lax.axis_size("gz") * lax.axis_size("gx")
    gram = gram_sum / total_cells
    factor_r, lower_inverse = chol_inv(gram)
    modes = split_modes(head, tail, lower_inverse)
    modes = modes.reshape(planes, rows_x, rows_z, snaps)
    return (modes, factor_r)


def solution(mesh):
    return jax.shard_map(
        local,
        mesh=mesh,
        in_specs=(P(None, "gx", "gz", None), P(None, "gx", "gz", None)),
        out_specs=(P(None, "gx", "gz", None), P()),
        check_vma=False,
    )
```

```python
import jax
import jax.numpy as jnp
from jax import lax
from jax.experimental import pallas as pl
from jax.experimental.pallas import tpu as pltpu
from jax.sharding import PartitionSpec as P

span_step = 0.75


def with_halo(cells, sides, width):
    for axis, dim in sides:
        count = lax.axis_size(axis)
        head = lax.slice_in_dim(cells, 0, width, axis=dim)
        tail = lax.slice_in_dim(cells, cells.shape[dim] - width, cells.shape[dim], axis=dim)
        cells = jnp.concatenate(
            [
                lax.ppermute(tail, axis, [(i, (i + 1) % count) for i in range(count)]),
                cells,
                lax.ppermute(head, axis, [((i + 1) % count, i) for i in range(count)]),
            ],
            axis=dim,
        )
    return cells


def ring_stages(size):
    stages, step = [], 1
    while step < size:
        if step * 2 == size and size == 8:
            stages.append([6, 7, 4, 5, 2, 3, 0, 1])
        elif step * 2 == size and size > 2:
            stages.append([size - 1 - p for p in range(size)])
        else:
            stages.append([p ^ step for p in range(size)])
        step *= 2
    return stages


def axis_stages(count, inner):
    if count % inner:
        inner = count
    outer = count // inner
    stages = [[i - i % inner + perm[i % inner] for i in range(count)] for perm in ring_stages(inner)]
    stages += [[perm[i // inner] * inner + i % inner for i in range(count)] for perm in ring_stages(outer)]
    return stages


def butterfly_sum(x, axes):
    for axis, inner in axes:
        count = lax.axis_size(axis)
        for partner in axis_stages(count, inner):
            x = x + lax.ppermute(x, axis, [(i, partner[i]) for i in range(count)])
    return x

def split(values):
    head32 = lax.reduce_precision(values, exponent_bits=8, mantissa_bits=7)
    return head32.astype(jnp.bfloat16), (values - head32).astype(jnp.bfloat16)


def split_gram(head, tail):
    def dot(a, b):
        return jnp.einsum("pcs,pct->pst", a, b, preferred_element_type=jnp.float32)

    cross = dot(head, tail)
    return dot(head, head) + (cross + jnp.swapaxes(cross, 1, 2)) + dot(tail, tail)


def split_modes(head, tail, inv_head, inv_tail):
    def dot(a, b):
        return jnp.einsum("pcs,pts->pct", a, b, preferred_element_type=jnp.float32)

    return dot(head, inv_head) + (dot(head, inv_tail) + dot(tail, inv_head))

def pack_pair(gram):
    n = gram.shape[-1]
    row = lax.broadcasted_iota(jnp.int32, (n, n), 0)
    col = lax.broadcasted_iota(jnp.int32, (n, n), 1)
    square = jnp.where(row <= col, gram[0], gram[1])
    diag = jnp.sum(jnp.where(row == col, gram[1], 0.0), axis=0, keepdims=True)
    pad = jnp.zeros((7, n), gram.dtype)
    return jnp.concatenate([square, diag, pad], axis=0)


def unpack_pair(packed):
    n = packed.shape[-1]
    square = packed[:n]
    diag = packed[n]
    row = lax.broadcasted_iota(jnp.int32, (n, n), 0)
    col = lax.broadcasted_iota(jnp.int32, (n, n), 1)
    flipped = square.T
    first = jnp.where(row <= col, square, flipped)
    second = jnp.where(row > col, square, jnp.where(row < col, flipped, jnp.diag(diag)))
    return jnp.stack([first, second])


def chol_inv_kernel(g_ref, rt_ref, head_ref, tail_ref, x_ref, s_ref):
    planes, n, _ = g_ref.shape
    s_ref[...] = g_ref[...]
    rr = lax.broadcasted_iota(jnp.int32, (n, n), 0)
    cc = lax.broadcasted_iota(jnp.int32, (n, n), 1)
    eye = jnp.where(rr == cc, 1.0, 0.0).astype(jnp.float32)
    for p in range(planes):
        x_ref[p] = eye
    lane = lax.broadcasted_iota(jnp.int32, (1, n), 1)
    pivot = [g_ref[p, 0:1, :] for p in range(planes)]
    for j in range(n):
        lo = (j // 8) * 8
        rows = lax.broadcasted_iota(jnp.int32, (n - lo, 1), 0) + lo
        for p in range(planes):
            rowj = pivot[p]
            root = jnp.sqrt(rowj[:, j:j + 1])
            inv = lax.rsqrt(rowj[:, j:j + 1])
            lrow = rowj * inv
            rt_ref[p, j:j + 1, :] = jnp.where(lane > j, lrow, jnp.where(lane == j, root, 0.0))
            if j + 1 < n:
                nxt = s_ref[p, j + 1:j + 2, :]
                pivot[p] = nxt - (nxt[:, j:j + 1] * inv) * lrow
            blk = s_ref[p, lo:, :]
            lcol = jnp.where(rows > j, blk[:, j:j + 1] * inv, 0.0)
            s_ref[p, lo:, :] = blk - lcol * lrow
            xrow = x_ref[p, j:j + 1, :] * inv
            xblk = x_ref[p, lo:, :]
            x_ref[p, lo:, :] = jnp.where(rows == j, xrow, xblk - lcol * xrow)
    for p in range(planes):
        inverse = x_ref[p]
        head = inverse.astype(jnp.bfloat16)
        head_ref[p] = head
        tail_ref[p] = (inverse - head.astype(jnp.float32)).astype(jnp.bfloat16)

def chol_inv(gram):
    planes, n, _ = gram.shape
    return pl.pallas_call(
        chol_inv_kernel,
        out_shape=(
            jax.ShapeDtypeStruct(gram.shape, jnp.float32),
            jax.ShapeDtypeStruct(gram.shape, jnp.bfloat16),
            jax.ShapeDtypeStruct(gram.shape, jnp.bfloat16),
        ),
        in_specs=[pl.BlockSpec(memory_space=pltpu.VMEM)],
        out_specs=(pl.BlockSpec(memory_space=pltpu.VMEM),) * 3,
        scratch_shapes=[pltpu.VMEM(gram.shape, jnp.float32)] * 2,
        compiler_params=pltpu.CompilerParams(allow_input_fusion=[True]),
    )(gram)


def local(u_field, w_field):
    planes, rows_x, rows_z, snaps = u_field.shape
    padded_u = with_halo(u_field, (("gz", 2),), 2).astype(jnp.float32)
    padded_w = with_halo(w_field, (("gx", 1),), 2).astype(jnp.float32)
    span_diff = 8.0 * (padded_u[:, :, 3:-1] - padded_u[:, :, 1:-3]) - (
        padded_u[:, :, 4:] - padded_u[:, :, :-4]
    )
    stream_diff = 8.0 * (padded_w[:, 3:-1] - padded_w[:, 1:-3]) - (
        padded_w[:, 4:] - padded_w[:, :-4]
    )
    vorticity = span_diff / (12.0 * span_step) - stream_diff / 12.0
    columns = vorticity.reshape(planes, rows_x * rows_z, snaps)
    head, tail = lax.optimization_barrier(split(columns))
    gram_local = split_gram(head, tail)
    if planes == 2:
        gram_sum = unpack_pair(butterfly_sum(pack_pair(gram_local), (("gx", 2), ("gz", 8))))
    else:
        gram_sum = butterfly_sum(gram_local, (("gx", 2), ("gz", 8)))
    total_cells = rows_x * rows_z * lax.axis_size("gz") * lax.axis_size("gx")
    gram = gram_sum / total_cells
    factor_r, inv_head, inv_tail = chol_inv(gram)
    modes = split_modes(head, tail, inv_head, inv_tail)
    modes = modes.reshape(planes, rows_x, rows_z, snaps)
    return (modes, factor_r)


def solution(mesh):
    return jax.shard_map(
        local,
        mesh=mesh,
        in_specs=(P(None, "gx", "gz", None), P(None, "gx", "gz", None)),
        out_specs=(P(None, "gx", "gz", None), P()),
        check_vma=False,
    )
```

```python
import jax
import jax.numpy as jnp
from jax import lax
from jax.experimental import pallas as pl
from jax.experimental.pallas import tpu as pltpu
from jax.sharding import PartitionSpec as P

span_step = 0.75


def with_halo(cells, sides, width):
    for axis, dim in sides:
        count = lax.axis_size(axis)
        head = lax.slice_in_dim(cells, 0, width, axis=dim)
        tail = lax.slice_in_dim(cells, cells.shape[dim] - width, cells.shape[dim], axis=dim)
        cells = jnp.concatenate(
            [
                lax.ppermute(tail, axis, [(i, (i + 1) % count) for i in range(count)]),
                cells,
                lax.ppermute(head, axis, [((i + 1) % count, i) for i in range(count)]),
            ],
            axis=dim,
        )
    return cells


def ring_stages(size):
    stages, step = [], 1
    while step < size:
        if step * 2 == size and size == 8:
            stages.append([6, 7, 4, 5, 2, 3, 0, 1])
        elif step * 2 == size and size > 2:
            stages.append([size - 1 - p for p in range(size)])
        else:
            stages.append([p ^ step for p in range(size)])
        step *= 2
    return stages


def axis_stages(count, inner):
    if count % inner:
        inner = count
    outer = count // inner
    stages = [[i - i % inner + perm[i % inner] for i in range(count)] for perm in ring_stages(inner)]
    stages += [[perm[i // inner] * inner + i % inner for i in range(count)] for perm in ring_stages(outer)]
    return stages


def butterfly_sum(x, axes):
    for axis, inner in axes:
        count = lax.axis_size(axis)
        for partner in axis_stages(count, inner):
            x = x + lax.ppermute(x, axis, [(i, partner[i]) for i in range(count)])
    return x

def split(values):
    head32 = lax.reduce_precision(values, exponent_bits=8, mantissa_bits=7)
    return head32.astype(jnp.bfloat16), (values - head32).astype(jnp.bfloat16)


def split_gram(head, tail):
    def dot(a, b):
        return jnp.einsum("pcs,pct->pst", a, b, preferred_element_type=jnp.float32)

    cross = dot(head, tail)
    return dot(head, head) + (cross + jnp.swapaxes(cross, 1, 2)) + dot(tail, tail)


def split_modes(head, tail, inv_head, inv_tail):
    def dot(a, b):
        return jnp.einsum("pcs,pts->pct", a, b, preferred_element_type=jnp.float32)

    return dot(head, inv_head) + (dot(head, inv_tail) + dot(tail, inv_head))

def pack_pair(gram):
    n = gram.shape[-1]
    row = lax.broadcasted_iota(jnp.int32, (n, n), 0)
    col = lax.broadcasted_iota(jnp.int32, (n, n), 1)
    square = jnp.where(row <= col, gram[0], gram[1])
    diag = jnp.sum(jnp.where(row == col, gram[1], 0.0), axis=0, keepdims=True)
    pad = jnp.zeros((7, n), gram.dtype)
    return jnp.concatenate([square, diag, pad], axis=0)


def unpack_pair(packed):
    n = packed.shape[-1]
    square = packed[:n]
    diag = packed[n]
    row = lax.broadcasted_iota(jnp.int32, (n, n), 0)
    col = lax.broadcasted_iota(jnp.int32, (n, n), 1)
    flipped = square.T
    first = jnp.where(row <= col, square, flipped)
    second = jnp.where(row > col, square, jnp.where(row < col, flipped, jnp.diag(diag)))
    return jnp.stack([first, second])


def chol_inv_kernel(g_ref, rt_ref, head_ref, tail_ref, x_ref, s_ref):
    planes, n, _ = g_ref.shape
    s_ref[...] = g_ref[...]
    rr = lax.broadcasted_iota(jnp.int32, (n, n), 0)
    cc = lax.broadcasted_iota(jnp.int32, (n, n), 1)
    eye = jnp.where(rr == cc, 1.0, 0.0).astype(jnp.float32)
    for p in range(planes):
        x_ref[p] = eye
    lane = lax.broadcasted_iota(jnp.int32, (1, n), 1)
    pivot = [g_ref[p, 0:1, :] for p in range(planes)]
    for j in range(n):
        lo = (j // 8) * 8
        rows = lax.broadcasted_iota(jnp.int32, (n - lo, 1), 0) + lo
        for p in range(planes):
            rowj = pivot[p]
            root = jnp.sqrt(rowj[:, j:j + 1])
            inv = lax.rsqrt(rowj[:, j:j + 1])
            lrow = rowj * inv
            rt_ref[p, j:j + 1, :] = jnp.where(lane > j, lrow, jnp.where(lane == j, root, 0.0))
            if j + 1 < n:
                nxt = s_ref[p, j + 1:j + 2, :]
                pivot[p] = nxt - (nxt[:, j:j + 1] * inv) * lrow
            blk = s_ref[p, lo:, :]
            lcol = jnp.where(rows > j, blk[:, j:j + 1] * inv, 0.0)
            s_ref[p, lo:, :] = blk - lcol * lrow
            xrow = x_ref[p, j:j + 1, :] * inv
            xblk = x_ref[p, lo:, :]
            x_ref[p, lo:, :] = jnp.where(rows == j, xrow, xblk - lcol * xrow)
    for p in range(planes):
        inverse = x_ref[p]
        head = inverse.astype(jnp.bfloat16)
        head_ref[p] = head
        tail_ref[p] = (inverse - head.astype(jnp.float32)).astype(jnp.bfloat16)

def chol_inv(gram):
    planes, n, _ = gram.shape
    return pl.pallas_call(
        chol_inv_kernel,
        out_shape=(
            jax.ShapeDtypeStruct(gram.shape, jnp.float32),
            jax.ShapeDtypeStruct(gram.shape, jnp.bfloat16),
            jax.ShapeDtypeStruct(gram.shape, jnp.bfloat16),
        ),
        in_specs=[pl.BlockSpec(memory_space=pltpu.VMEM)],
        out_specs=(pl.BlockSpec(memory_space=pltpu.VMEM),) * 3,
        scratch_shapes=[pltpu.VMEM(gram.shape, jnp.float32)] * 2,
        compiler_params=pltpu.CompilerParams(allow_input_fusion=[True]),
    )(gram)


def local(u_field, w_field):
    planes, rows_x, rows_z, snaps = u_field.shape
    padded_w = with_halo(w_field, (("gx", 1),), 2).astype(jnp.float32)
    w_edges = (w_field[:, :2], w_field[:, -2:])
    u_field = lax.optimization_barrier((w_edges, u_field))[1]
    padded_u = with_halo(u_field, (("gz", 2),), 2).astype(jnp.float32)
    span_diff = 8.0 * (padded_u[:, :, 3:-1] - padded_u[:, :, 1:-3]) - (
        padded_u[:, :, 4:] - padded_u[:, :, :-4]
    )
    stream_diff = 8.0 * (padded_w[:, 3:-1] - padded_w[:, 1:-3]) - (
        padded_w[:, 4:] - padded_w[:, :-4]
    )
    vorticity = span_diff / (12.0 * span_step) - stream_diff / 12.0
    columns = vorticity.reshape(planes, rows_x * rows_z, snaps)
    head, tail = lax.optimization_barrier(split(columns))
    gram_local = split_gram(head, tail)
    if planes == 2:
        gram_sum = unpack_pair(butterfly_sum(pack_pair(gram_local), (("gx", 2), ("gz", 8))))
    else:
        gram_sum = butterfly_sum(gram_local, (("gx", 2), ("gz", 8)))
    total_cells = rows_x * rows_z * lax.axis_size("gz") * lax.axis_size("gx")
    gram = gram_sum / total_cells
    factor_r, inv_head, inv_tail = chol_inv(gram)
    modes = split_modes(head, tail, inv_head, inv_tail)
    modes = modes.reshape(planes, rows_x, rows_z, snaps)
    return (modes, factor_r)


def solution(mesh):
    return jax.shard_map(
        local,
        mesh=mesh,
        in_specs=(P(None, "gx", "gz", None), P(None, "gx", "gz", None)),
        out_specs=(P(None, "gx", "gz", None), P()),
        check_vma=False,
    )
```
